512 devices in a mesh: req: 128 (over y, z, core), mlp: 4 (over x).
Axes of the slice: x: 4, y: 8, z: 8, core: 2. Of those that a mesh axis runs over, the one named last changes fastest.
Arguments:
- residual: bfloat16 [32768, 2048], P('req'), may hold values from -20 to 20
- query_rows: bfloat16 [32768, 2048], P('req', 'mlp'), may hold values from -6 to 6
- value_rows: bfloat16 [32768, 2048], P('req', 'mlp'), may hold values from -6 to 6
- forget_logit: float32 [32768, 2048], P('req', 'mlp'), may hold values from 0 to 40
- slot_kind: int32 [32768], P('req'), may hold values from 0 to 2, as said below
- head_gain: float32 [2048], P('mlp'), may hold values from 0.1 to 1.9
- out_weight: bfloat16 [2048, 2048], P('mlp', 'req'), may hold values from -0.125 to 0.125
- ffn_gain: float32 [2048], replicated, may hold values from 0.1 to 1.9
- gate_weight: bfloat16 [2048, 3072], P('req', 'mlp'), may hold values from -0.125 to 0.125
- up_weight: bfloat16 [2048, 3072], P('req', 'mlp'), may hold values from -0.125 to 0.125
- down_weight: bfloat16 [3072, 2048], P('mlp', 'req'), may hold values from -0.109375 to 0.109375
Outputs:
- layer_out: bfloat16 [32768, 2048], P('req', 'mlp')
The draws below stay inside these ranges and needn't reach their ends.
Inputs may be any that keep to these rules, and one draw needn't show every extreme that they name: `slot_kind`: slots 0 to 24575 hold one prompt: slot 0 has kind 2, the others kind 1. Every other block of 256 slots holds short requests packed from its first slot, then empty slots; a short request has at most 32 tokens, the first request of each such block exactly 32. Over all 32768 slots exactly 26624 are live.
All inputs are finite; a program needn't handle non-finite values.
Results may differ from the reference program's by a relative error of at most 0.0163.
Values may be sent and summed in bfloat16 or wider, within the bound.
No kernel may reach another device: no remote copies, remote signals or barrier semaphores. Data moves between devices by JAX's collectives and lax.ppermute only.
A program may use at most 128 MiB of HBM per device.

```python
import jax
import jax.numpy as jnp
from jax import lax

MODEL_WIDTH = 2048
HEADS = 16
HEAD = 128
FF = 3072
SPAN = 32
SHORT_MAX = 32
SLOTS = 256
TOKEN_SLOTS = 32768
LONG = 24576
N_MLP = 4


def draw_slot_kind(key, part):
    key_len = jax.random.fold_in(key, 11)
    key_cut = jax.random.fold_in(key, 12)
    slot_numbers = jnp.arange(TOKEN_SLOTS)
    inside = slot_numbers % SLOTS
    pair_count = max((TOKEN_SLOTS - LONG) // (2 * SLOTS), 1)
    shifts = jax.random.randint(key_len, (pair_count,), 0, SLOTS // 8 + 1)
    short_dev = jnp.maximum(slot_numbers - LONG, 0) // SLOTS
    pair_id = jnp.minimum(short_dev // 2, pair_count - 1)
    sign_val = 1 - 2 * (short_dev % 2)
    length = SLOTS // 4 + sign_val * shifts[pair_id]
    live_short = inside < length
    random_cut = jax.random.randint(key_cut, (TOKEN_SLOTS,), 0, 12) == 0
    cut_here = (inside == 0) | (inside == SHORT_MAX) | (inside > SHORT_MAX) & ((inside % SHORT_MAX == 0) | random_cut)
    short_kind = jnp.where(live_short, jnp.where(cut_here, 2, 1), 0)
    long_kind = jnp.where(slot_numbers == 0, 2, 1)
    return jnp.where(slot_numbers < LONG, long_kind, short_kind).astype(jnp.int32)


def draw_forget_logit(key, part):
    key_rows = [jax.random.fold_in(key, 21 + index) for index in range(6)]
    heads_all = MODEL_WIDTH // HEAD
    slow_share = 0.5
    head_slow = jax.random.uniform(key_rows[0], (heads_all,)) < slow_share
    channel_slow = head_slow[jnp.arange(MODEL_WIDTH) // HEAD]
    spread = jax.random.uniform(key_rows[1], (MODEL_WIDTH,))
    rate_slow = jnp.exp(jnp.log(0.2 / LONG) + spread * jnp.log(5.0))
    rate_fast = jnp.exp(jnp.log(1.0 / 400.0) + spread * jnp.log(400.0 / 25.0))
    base_rate = jnp.where(channel_slow, rate_slow, rate_fast)
    slot_numbers = jnp.arange(TOKEN_SLOTS)
    device_factor = jnp.exp(jax.random.uniform(key_rows[2], (TOKEN_SLOTS // SLOTS, MODEL_WIDTH), minval=-0.7, maxval=0.7))
    token_factor = jnp.exp(jax.random.uniform(key_rows[3], (TOKEN_SLOTS, MODEL_WIDTH), minval=-0.3, maxval=0.3))
    decay_speed = jnp.minimum(base_rate[None] * device_factor[slot_numbers // SLOTS] * token_factor, 0.1)
    spike_rows = jax.random.randint(key_rows[4], (8,), 0, TOKEN_SLOTS)
    spike_flags = jnp.any(slot_numbers[:, None] == spike_rows[None, :], axis=1)
    spike_rate = jax.random.uniform(key_rows[5], (TOKEN_SLOTS, MODEL_WIDTH), minval=0.2, maxval=0.5)
    decay_speed = jnp.where(spike_flags[:, None], spike_rate, decay_speed)
    return (jnp.log1p(-decay_speed) - jnp.log(decay_speed)).astype(jnp.float32)


def draw_residual(key, part):
    key_val = jax.random.fold_in(key, 31)
    key_row = jax.random.fold_in(key, 32)
    row_scale = jnp.exp(jnp.log(0.3) + jax.random.uniform(key_row, (TOKEN_SLOTS, 1)) * jnp.log(10.0))
    values = jnp.clip(jax.random.normal(key_val, (TOKEN_SLOTS, MODEL_WIDTH)), -6.0, 6.0)
    return jnp.clip(values * row_scale, -20.0, 20.0).astype(jnp.bfloat16)


def shard_levels(key, shape, cuts, low, largest):
    gain, own = 1.0, jax.random.fold_in(key, 6)
    for position, parts in cuts:
        draws = jnp.exp(jax.random.uniform(jax.random.fold_in(own, position), (parts,), jnp.float32, low / len(cuts), largest / len(cuts)))
        gain = gain * jnp.repeat(draws, shape[position] // parts).reshape([-1 if axis == position else 1 for axis in range(len(shape))])
    return gain


def normal_values(rng, shape, scale, reach, split=(), kind=jnp.bfloat16):
    level = shard_levels(rng, shape, split, -0.22, 0.18) if split else 1.0
    values = jax.random.normal(rng, shape, jnp.float32) * scale * level
    return jnp.minimum(jnp.maximum(values, -reach), reach).astype(kind)


def setup_inputs(seed: int = 0) -> dict:
    key_of = jax.random.split(jax.random.key(seed), 12)
    return {
        "residual": draw_residual(jax.random.fold_in(key_of[11], 71), 0),
        "query_rows": normal_values(key_of[1], (TOKEN_SLOTS, MODEL_WIDTH), 1.0, 6.0, ((0, 128), (1, 4))),
        "value_rows": normal_values(key_of[2], (TOKEN_SLOTS, MODEL_WIDTH), 1.0, 6.0, ((0, 128), (1, 4))),
        "forget_logit": draw_forget_logit(jax.random.fold_in(key_of[11], 71), 0),
        "slot_kind": draw_slot_kind(jax.random.fold_in(key_of[11], 71), 0),
        "head_gain": jnp.clip(1.0 + 0.18 * jax.random.normal(key_of[5], (MODEL_WIDTH,), jnp.float32), 0.1, 1.9),
        "out_weight": normal_values(key_of[6], (MODEL_WIDTH, MODEL_WIDTH), MODEL_WIDTH ** -0.5, 0.125, ((0, 4), (1, 128))),
        "ffn_gain": jnp.clip(1.0 + 0.18 * jax.random.normal(key_of[7], (MODEL_WIDTH,), jnp.float32), 0.1, 1.9),
        "gate_weight": normal_values(key_of[8], (MODEL_WIDTH, FF), MODEL_WIDTH ** -0.5, 0.125, ((0, 128), (1, 4))),
        "up_weight": normal_values(key_of[9], (MODEL_WIDTH, FF), MODEL_WIDTH ** -0.5, 0.125, ((0, 128), (1, 4))),
        "down_weight": normal_values(key_of[10], (FF, MODEL_WIDTH), FF ** -0.5, 0.109375, ((0, 4), (1, 128))),
    }


def span_step(passed_state, pieces):
    query_block, key_block, value_block, g_block = pieces
    top_precision = lax.Precision.HIGHEST
    inside_block_term = jnp.cumsum(g_block, axis=0)
    between_blocks_term = jnp.einsum('owu,wuj->owj', query_block * jnp.exp(inside_block_term), passed_state, precision=top_precision)
    length = g_block.shape[0]
    causal = jnp.arange(length)[:, None] >= jnp.arange(length)[None, :]
    causal = causal[:, :, None, None]
    gap_log = jnp.where(causal, inside_block_term[:, None] - inside_block_term[None, :], 0.0)
    decay_pairs = jnp.where(causal, jnp.exp(gap_log), 0.0)
    scores = jnp.einsum('tnk,tsnk->tsn', query_block, decay_pairs * key_block[None], precision=top_precision)
    intra_part = jnp.einsum('tsn,snv->tnv', scores, value_block, precision=top_precision)
    final_decay_sum = inside_block_term[-1]
    updated_state = jnp.exp(final_decay_sum)[:, :, None] * passed_state + jnp.einsum('weq,wel->eql', key_block * jnp.exp(final_decay_sum[None] - inside_block_term), value_block, precision=top_precision)
    return (updated_state, between_blocks_term + intra_part)

def reference(residual, query_rows, value_rows, forget_logit, slot_kind, head_gain, out_weight, ffn_gain, gate_weight, up_weight, down_weight):
    live_mask = slot_kind > 0
    first_mask = slot_kind == 2
    log_forget = jnp.where(first_mask[:, None], -80.0, jnp.where(live_mask[:, None], -jax.nn.softplus(-forget_logit), 0.0))
    key_gate = jnp.where(live_mask[:, None], jax.nn.sigmoid(-forget_logit), 0.0)
    shape4 = (TOKEN_SLOTS // SPAN, SPAN, HEADS, HEAD)
    q_all = query_rows.astype(jnp.float32).reshape(shape4)
    v_all = value_rows.astype(jnp.float32).reshape(shape4)
    k_all = key_gate.astype(jnp.float32).reshape(shape4)
    g_all = log_forget.astype(jnp.float32).reshape(shape4)
    start_state = jnp.zeros((HEADS, HEAD, HEAD), jnp.float32)
    _, recurrent = lax.scan(span_step, start_state, (q_all, k_all, v_all, g_all))
    recurrent = recurrent.reshape(TOKEN_SLOTS, HEADS, HEAD)
    mean_sq = lax.optimization_barrier(jnp.mean(recurrent * recurrent, axis=-1, keepdims=True))
    head_normed = (recurrent / jnp.sqrt(mean_sq + 1e-06) * head_gain.reshape(HEADS, HEAD)).astype(jnp.bfloat16)
    head_normed = head_normed.reshape(TOKEN_SLOTS, MODEL_WIDTH)
    group_width = MODEL_WIDTH // N_MLP
    mixed_sum = jnp.zeros((TOKEN_SLOTS, MODEL_WIDTH), jnp.float32)
    for group in range(N_MLP):
        lo_col = group * group_width
        partial_rows = jnp.dot(head_normed[:, lo_col:lo_col + group_width], out_weight[lo_col:lo_col + group_width], preferred_element_type=jnp.float32).astype(jnp.bfloat16)
        mixed_sum = mixed_sum + lax.optimization_barrier(partial_rows).astype(jnp.float32)
    stream = (residual.astype(jnp.float32) + mixed_sum).astype(jnp.bfloat16)

    def ffn_block(inputs):
        stream_rows, live_rows = inputs
        rows_f = stream_rows.astype(jnp.float32)
        ffn_in = (rows_f / jnp.sqrt(lax.optimization_barrier(jnp.mean(rows_f * rows_f, axis=-1, keepdims=True)) + 1e-05) * ffn_gain).astype(jnp.bfloat16)
        gate_acc = jnp.dot(ffn_in, gate_weight, preferred_element_type=jnp.float32)
        up_acc = jnp.dot(ffn_in, up_weight, preferred_element_type=jnp.float32)
        hidden = (jax.nn.silu(gate_acc) * up_acc).astype(jnp.bfloat16)
        ffn_out = jnp.dot(hidden, down_weight, preferred_element_type=jnp.float32)
        result = (rows_f + ffn_out).astype(jnp.bfloat16)
        return jnp.where(live_rows[:, None], result, jnp.zeros_like(result))
    blocks = TOKEN_SLOTS // SLOTS
    layer_out = lax.map(ffn_block, (stream.reshape(blocks, SLOTS, MODEL_WIDTH), live_mask.reshape(blocks, SLOTS)))
    return layer_out.reshape(TOKEN_SLOTS, MODEL_WIDTH)
```

```python
import jax
import jax.numpy as jnp
from jax import lax
from jax.sharding import Mesh, PartitionSpec as P

HEAD = 128
SPAN = 32
TOP = lax.Precision.HIGHEST
REQ = ("rp", "rc")


def span_step(passed_state, pieces):
    query_block, key_block, value_block, g_block = pieces
    inside_block_term = jnp.cumsum(g_block, axis=0)
    between_blocks_term = jnp.einsum(
        "owu,wuj->owj",
        query_block * jnp.exp(inside_block_term),
        passed_state,
        precision=TOP,
    )
    length = g_block.shape[0]
    causal = jnp.arange(length)[:, None] >= jnp.arange(length)[None, :]
    causal = causal[:, :, None, None]
    gap_log = jnp.where(causal, inside_block_term[:, None] - inside_block_term[None, :], 0.0)
    decay_pairs = jnp.where(causal, jnp.exp(gap_log), 0.0)
    scores = jnp.einsum("tnk,tsnk->tsn", query_block, decay_pairs * key_block[None], precision=TOP)
    intra_part = jnp.einsum("tsn,snv->tnv", scores, value_block, precision=TOP)
    final_decay_sum = inside_block_term[-1]
    updated_state = jnp.exp(final_decay_sum)[:, :, None] * passed_state + jnp.einsum(
        "weq,wel->eql",
        key_block * jnp.exp(final_decay_sum[None] - inside_block_term),
        value_block,
        precision=TOP,
    )
    return (updated_state, between_blocks_term + intra_part)


def compose(earlier, later):
    return (earlier[0] * later[0], later[0][:, :, None] * earlier[1] + later[1])


def carried_in(decay, state, count):
    place = lax.axis_index(REQ)
    ones = jnp.ones_like(decay)
    decay, state = lax.ppermute((decay, state), REQ, [(i, i + 1) for i in range(count - 1)])
    decay = jnp.where(place == 0, ones, decay)
    hop = 1
    while hop < count:
        got = lax.ppermute((decay, state), REQ, [(i, i + hop) for i in range(count - hop)])
        joined = compose(got, (decay, state))
        take = place >= hop
        decay = jnp.where(take, joined[0], decay)
        state = jnp.where(take, joined[1], state)
        hop *= 2
    return state


def mlp_sum(parts, n_mlp):
    rows, width = parts.shape
    blocks = parts.reshape(rows, n_mlp, width // n_mlp).transpose(1, 0, 2)
    got = lax.all_to_all(blocks, "mlp", 0, 0)
    return jnp.sum(got.astype(jnp.float32), axis=0)


def mlp_gather(cols, n_mlp):
    rows, width = cols.shape
    sent = jnp.broadcast_to(cols[None], (n_mlp, rows, width))
    got = lax.all_to_all(sent, "mlp", 0, 0)
    return got.transpose(1, 0, 2).reshape(rows, n_mlp * width)


def on_device(
    residual,
    query_rows,
    value_rows,
    forget_logit,
    slot_kind,
    head_gain,
    out_weight,
    ffn_gain,
    gate_weight,
    up_weight,
    down_weight,
    *,
    n_pairs,
    n_mlp,
):
    slot_total = residual.shape[0]
    quarter = query_rows.shape[1]
    heads_here = quarter // HEAD
    hidden_here = gate_weight.shape[1]

    packed = jnp.concatenate([gate_weight, up_weight, out_weight.T, down_weight.T], axis=1)
    over_chips = lax.all_gather(packed, "rp", axis=0)
    over_cores = lax.all_gather(over_chips, "rc", axis=0)
    rows_each = packed.shape[0]
    full = over_cores.transpose(1, 0, 2, 3).reshape(2 * n_pairs * rows_each, packed.shape[1])
    gate_full = full[:, :hidden_here]
    up_full = full[:, hidden_here:2 * hidden_here]
    out_t = full[:, 2 * hidden_here:2 * hidden_here + quarter]
    down_t = full[:, 2 * hidden_here + quarter:]

    live_mask = slot_kind > 0
    first_mask = slot_kind == 2
    log_forget = jnp.where(
        first_mask[:, None],
        -80.0,
        jnp.where(live_mask[:, None], -jax.nn.softplus(-forget_logit), 0.0),
    )
    key_gate = jnp.where(live_mask[:, None], jax.nn.sigmoid(-forget_logit), 0.0)
    shape3 = (slot_total, heads_here, HEAD)
    q3 = query_rows.astype(jnp.float32).reshape(shape3)
    v3 = value_rows.astype(jnp.float32).reshape(shape3)
    k3 = key_gate.reshape(shape3)
    g3 = log_forget.reshape(shape3)

    running = jnp.cumsum(g3, axis=0)
    total = running[-1]
    end_state = jnp.einsum(
        "thk,thv->hkv", k3 * jnp.exp(total[None] - running), v3, precision=TOP
    )
    state_in = carried_in(jnp.exp(total), end_state, 2 * n_pairs)

    shape4 = (slot_total // SPAN, SPAN, heads_here, HEAD)
    zero_state = jnp.zeros((heads_here, HEAD, HEAD), jnp.float32)
    _, local_out = lax.scan(
        span_step,
        zero_state,
        (q3.reshape(shape4), k3.reshape(shape4), v3.reshape(shape4), g3.reshape(shape4)),
    )
    heads_out = local_out.reshape(shape3) + jnp.einsum(
        "thk,hkv->thv", q3 * jnp.exp(running), state_in, precision=TOP
    )
    mean_sq = jnp.mean(heads_out * heads_out, axis=-1, keepdims=True)
    head_normed = (
        heads_out / jnp.sqrt(mean_sq + 1e-06) * head_gain.reshape(heads_here, HEAD)
    ).astype(jnp.bfloat16)
    head_normed = head_normed.reshape(slot_total, quarter)
    partial_rows = lax.dot_general(
        head_normed, out_t, (((1,), (1,)), ((), ())), preferred_element_type=jnp.float32
    ).astype(jnp.bfloat16)
    mixed_cols = mlp_sum(partial_rows, n_mlp)
    my_cols = lax.axis_index("mlp") * quarter
    own_res = lax.dynamic_slice_in_dim(residual, my_cols, quarter, 1).astype(jnp.float32)
    stream_cols = (own_res + mixed_cols).astype(jnp.bfloat16)
    stream = mlp_gather(stream_cols, n_mlp)

    rows_f = stream.astype(jnp.float32)
    ffn_in = (
        rows_f / jnp.sqrt(jnp.mean(rows_f * rows_f, axis=-1, keepdims=True) + 1e-05) * ffn_gain
    ).astype(jnp.bfloat16)
    gate_acc = jnp.dot(ffn_in, gate_full, preferred_element_type=jnp.float32)
    up_acc = jnp.dot(ffn_in, up_full, preferred_element_type=jnp.float32)
    hidden = (jax.nn.silu(gate_acc) * up_acc).astype(jnp.bfloat16)
    terms = lax.dot_general(
        hidden, down_t, (((1,), (1,)), ((), ())), preferred_element_type=jnp.float32
    ).astype(jnp.bfloat16)
    ffn_out = mlp_sum(terms, n_mlp)
    result = (stream_cols.astype(jnp.float32) + ffn_out).astype(jnp.bfloat16)
    return jnp.where(live_mask[:, None], result, jnp.zeros_like(result))


def solution(mesh):
    n_req = mesh.shape["req"]
    n_mlp = mesh.shape["mlp"]
    n_pairs = n_req // 2
    split = Mesh(mesh.devices.reshape(n_pairs, 2, n_mlp), ("rp", "rc", "mlp"))

    def body(*args):
        return on_device(*args, n_pairs=n_pairs, n_mlp=n_mlp)

    return jax.shard_map(
        body,
        mesh=split,
        in_specs=(
            P(REQ, None),
            P(REQ, "mlp"),
            P(REQ, "mlp"),
            P(REQ, "mlp"),
            P(REQ),
            P("mlp"),
            P("mlp", REQ),
            P(),
            P(REQ, "mlp"),
            P(REQ, "mlp"),
            P("mlp", REQ),
        ),
        out_specs=P(REQ, "mlp"),
        check_vma=False,
    )
```

```python
import jax
import jax.numpy as jnp
from jax import lax
from jax.sharding import Mesh, PartitionSpec as P

HEAD = 128
SPAN = 32
TOP = lax.Precision.HIGHEST
REQ = ("rp", "rc")


def compose(earlier, later):
    decay = later[:, HEAD:, :]
    joined = decay.transpose(0, 2, 1) * earlier[:, :HEAD, :] + later[:, :HEAD, :]
    return jnp.concatenate([joined, earlier[:, HEAD:, :] * decay], axis=1)


def carried_in(decay, state, count):
    place = lax.axis_index(REQ)
    packed = jnp.concatenate([state, decay[:, None, :]], axis=1)
    hop = 1
    while hop < count:
        got = lax.ppermute(packed, REQ, [(i, i + hop) for i in range(count - hop)])
        packed = jnp.where(place >= hop, compose(got, packed), packed)
        hop *= 2
    shifted = lax.ppermute(packed, REQ, [(i, i + 1) for i in range(count - 1)])
    return shifted[:, :HEAD, :]


def mlp_sum(parts, n_mlp):
    rows, width = parts.shape
    blocks = parts.reshape(rows, n_mlp, width // n_mlp).transpose(1, 0, 2)
    got = lax.all_to_all(blocks, "mlp", 0, 0)
    return jnp.sum(got.astype(jnp.float32), axis=0)


def mlp_gather(cols, n_mlp):
    rows, width = cols.shape
    sent = jnp.broadcast_to(cols[None], (n_mlp, rows, width))
    got = lax.all_to_all(sent, "mlp", 0, 0)
    return got.transpose(1, 0, 2).reshape(rows, n_mlp * width)


def gather_rows(piece, n_pairs):
    over_chips = lax.all_gather(piece, "rp", axis=0)
    sent = jnp.broadcast_to(over_chips[None], (2,) + over_chips.shape)
    over_cores = lax.all_to_all(sent, "rc", 0, 0)
    return over_cores.reshape(2 * n_pairs * piece.shape[0], piece.shape[1])


def to_natural(cols, n_pairs):
    rows, width = cols.shape
    return cols.reshape(rows, 2, n_pairs, -1).transpose(0, 2, 1, 3).reshape(rows, width)


def to_gathered(cols, n_pairs):
    rows, width = cols.shape
    return cols.reshape(rows, n_pairs, 2, -1).transpose(0, 2, 1, 3).reshape(rows, width)


def on_device(
    residual,
    query_rows,
    value_rows,
    forget_logit,
    slot_kind,
    head_gain,
    out_weight,
    ffn_gain,
    gate_weight,
    up_weight,
    down_weight,
    *,
    n_pairs,
    n_mlp,
):
    slot_total = residual.shape[0]
    quarter = query_rows.shape[1]
    heads_here = quarter // HEAD
    hidden_here = gate_weight.shape[1]

    out_t = gather_rows(out_weight.T, n_pairs)
    rest = gather_rows(jnp.concatenate([gate_weight, up_weight, down_weight.T], axis=1), n_pairs)
    gate_full = rest[:, :hidden_here]
    up_full = rest[:, hidden_here:2 * hidden_here]
    down_t = rest[:, 2 * hidden_here:]

    live_mask = slot_kind > 0
    first_mask = slot_kind == 2
    log_forget = jnp.where(
        first_mask[:, None],
        -80.0,
        jnp.where(live_mask[:, None], -jax.nn.softplus(-forget_logit), 0.0),
    )
    key_gate = jnp.where(live_mask[:, None], jax.nn.sigmoid(-forget_logit), 0.0)
    shape3 = (slot_total, heads_here, HEAD)
    q3 = query_rows.astype(jnp.float32).reshape(shape3)
    v3 = value_rows.astype(jnp.float32).reshape(shape3)
    k3 = key_gate.reshape(shape3)
    g3 = log_forget.reshape(shape3)

    spans = slot_total // SPAN
    shape4 = (spans, SPAN, heads_here, HEAD)
    q4 = q3.reshape(shape4)
    k4 = k3.reshape(shape4)
    v4 = v3.reshape(shape4)
    inside = jnp.cumsum(g3.reshape(shape4), axis=1)
    span_total = inside[:, -1]
    span_end = jnp.cumsum(span_total, axis=0)
    span_start = span_end - span_total
    span_state = jnp.einsum(
        "cshk,cshv->chkv", k4 * jnp.exp(span_total[:, None] - inside), v4, precision=TOP
    )
    end_state = jnp.einsum(
        "chk,chkv->hkv", jnp.exp(span_end[-1][None] - span_end), span_state, precision=TOP
    )
    state_in = carried_in(jnp.exp(span_end[-1]), end_state, 2 * n_pairs)

    causal = (jnp.arange(SPAN)[:, None] >= jnp.arange(SPAN)[None, :])[None, :, :, None, None]
    gap_log = jnp.where(causal, inside[:, :, None] - inside[:, None, :], 0.0)
    decay_pairs = jnp.where(causal, jnp.exp(gap_log), 0.0)
    scores = jnp.einsum("ctnk,ctsnk->ctsn", q4, decay_pairs * k4[:, None], precision=TOP)
    intra = jnp.einsum("ctsn,csnv->ctnv", scores, v4, precision=TOP)
    earlier = (jnp.arange(spans)[:, None] > jnp.arange(spans)[None, :])[:, :, None, None]
    weights = jnp.where(
        earlier, jnp.exp(jnp.where(earlier, span_start[:, None] - span_end[None, :], 0.0)), 0.0
    )
    local_in = jnp.einsum("cdhk,dhkv->chkv", weights, span_state, precision=TOP)
    local_out = intra + jnp.einsum("cthk,chkv->cthv", q4 * jnp.exp(inside), local_in, precision=TOP)
    running = inside + span_start[:, None]
    heads_out = local_out + jnp.einsum("cthk,hkv->cthv", q4 * jnp.exp(running), state_in, precision=TOP)
    heads_out = heads_out.reshape(shape3)
    mean_sq = jnp.mean(heads_out * heads_out, axis=-1, keepdims=True)
    head_normed = (
        heads_out / jnp.sqrt(mean_sq + 1e-06) * head_gain.reshape(heads_here, HEAD)
    ).astype(jnp.bfloat16)
    head_normed = head_normed.reshape(slot_total, quarter)
    partial_rows = to_natural(lax.dot_general(
        head_normed, out_t, (((1,), (1,)), ((), ())), preferred_element_type=jnp.float32
    ).astype(jnp.bfloat16), n_pairs)
    mixed_cols = mlp_sum(partial_rows, n_mlp)
    my_cols = lax.axis_index("mlp") * quarter
    own_res = lax.dynamic_slice_in_dim(residual, my_cols, quarter, 1).astype(jnp.float32)
    stream_cols = (own_res + mixed_cols).astype(jnp.bfloat16)
    stream = mlp_gather(stream_cols, n_mlp)

    rows_f = stream.astype(jnp.float32)
    ffn_in = (
        rows_f / jnp.sqrt(jnp.mean(rows_f * rows_f, axis=-1, keepdims=True) + 1e-05) * ffn_gain
    ).astype(jnp.bfloat16)
    ffn_in = to_gathered(ffn_in, n_pairs)
    gate_acc = jnp.dot(ffn_in, gate_full, preferred_element_type=jnp.float32)
    up_acc = jnp.dot(ffn_in, up_full, preferred_element_type=jnp.float32)
    hidden = (jax.nn.silu(gate_acc) * up_acc).astype(jnp.bfloat16)
    terms = to_natural(lax.dot_general(
        hidden, down_t, (((1,), (1,)), ((), ())), preferred_element_type=jnp.float32
    ).astype(jnp.bfloat16), n_pairs)
    ffn_out = mlp_sum(terms, n_mlp)
    result = (stream_cols.astype(jnp.float32) + ffn_out).astype(jnp.bfloat16)
    return jnp.where(live_mask[:, None], result, jnp.zeros_like(result))


def solution(mesh):
    n_req = mesh.shape["req"]
    n_mlp = mesh.shape["mlp"]
    n_pairs = n_req // 2
    split = Mesh(mesh.devices.reshape(n_pairs, 2, n_mlp), ("rp", "rc", "mlp"))

    def body(*args):
        return on_device(*args, n_pairs=n_pairs, n_mlp=n_mlp)

    return jax.shard_map(
        body,
        mesh=split,
        in_specs=(
            P(REQ, None),
            P(REQ, "mlp"),
            P(REQ, "mlp"),
            P(REQ, "mlp"),
            P(REQ),
            P("mlp"),
            P("mlp", REQ),
            P(),
            P(REQ, "mlp"),
            P(REQ, "mlp"),
            P("mlp", REQ),
        ),
        out_specs=P(REQ, "mlp"),
        check_vma=False,
    )
```

```python
import jax
import jax.numpy as jnp
from jax import lax
from jax.sharding import Mesh, PartitionSpec as P

HEAD = 128
SPAN = 32
TOP = lax.Precision.HIGHEST
REQ = ("rp", "rc")


def compose(earlier, later):
    decay = later[:, HEAD:, :]
    joined = decay.transpose(0, 2, 1) * earlier[:, :HEAD, :] + later[:, :HEAD, :]
    return jnp.concatenate([joined, earlier[:, HEAD:, :] * decay], axis=1)


def carried_in(decay, state, count):
    place = lax.axis_index(REQ)
    packed = jnp.concatenate([state, decay[:, None, :]], axis=1)
    hop = 1
    while hop < count:
        got = lax.ppermute(packed, REQ, [(i, i + hop) for i in range(count - hop)])
        packed = jnp.where(place >= hop, compose(got, packed), packed)
        hop *= 2
    shifted = lax.ppermute(packed, REQ, [(i, i + 1) for i in range(count - 1)])
    return shifted[:, :HEAD, :]


def mlp_sum(parts, n_mlp):
    rows, width = parts.shape
    blocks = parts.reshape(rows, n_mlp, width // n_mlp).transpose(1, 0, 2)
    got = lax.all_to_all(blocks, "mlp", 0, 0)
    return jnp.sum(got.astype(jnp.float32), axis=0)


def mlp_gather(cols, n_mlp):
    rows, width = cols.shape
    sent = jnp.broadcast_to(cols[None], (n_mlp, rows, width))
    got = lax.all_to_all(sent, "mlp", 0, 0)
    return got.transpose(1, 0, 2).reshape(rows, n_mlp * width)


def gather_rows(piece, n_pairs):
    over_chips = lax.all_gather(piece, "rp", axis=0)
    sent = jnp.broadcast_to(over_chips[None], (2,) + over_chips.shape)
    over_cores = lax.all_to_all(sent, "rc", 0, 0)
    return over_cores.reshape(2 * n_pairs * piece.shape[0], piece.shape[1])


def to_natural(cols, n_pairs):
    rows, width = cols.shape
    return cols.reshape(rows, 2, n_pairs, -1).transpose(0, 2, 1, 3).reshape(rows, width)


def to_gathered(cols, n_pairs):
    rows, width = cols.shape
    return cols.reshape(rows, n_pairs, 2, -1).transpose(0, 2, 1, 3).reshape(rows, width)


def on_device(
    residual,
    query_rows,
    value_rows,
    forget_logit,
    slot_kind,
    head_gain,
    out_weight,
    ffn_gain,
    gate_weight,
    up_weight,
    down_weight,
    *,
    n_pairs,
    n_mlp,
):
    slot_total = residual.shape[0]
    quarter = query_rows.shape[1]
    heads_here = quarter // HEAD
    hidden_here = gate_weight.shape[1]

    quarter_cols = 2 * hidden_here
    full = gather_rows(
        jnp.concatenate([gate_weight, up_weight, out_weight.T, down_weight.T], axis=1), n_pairs
    )
    gate_full = full[:, :hidden_here]
    up_full = full[:, hidden_here:quarter_cols]
    out_t = full[:, quarter_cols:quarter_cols + quarter]
    down_t = full[:, quarter_cols + quarter:]

    live_mask = slot_kind > 0
    first_mask = slot_kind == 2
    log_forget = jnp.where(
        first_mask[:, None],
        -80.0,
        jnp.where(live_mask[:, None], -jax.nn.softplus(-forget_logit), 0.0),
    )
    key_gate = jnp.where(live_mask[:, None], jax.nn.sigmoid(-forget_logit), 0.0)
    shape3 = (slot_total, heads_here, HEAD)
    q3 = query_rows.astype(jnp.float32).reshape(shape3)
    v3 = value_rows.astype(jnp.float32).reshape(shape3)
    k3 = key_gate.reshape(shape3)
    g3 = log_forget.reshape(shape3)

    spans = slot_total // SPAN
    shape4 = (spans, SPAN, heads_here, HEAD)
    q4 = q3.reshape(shape4)
    k4 = k3.reshape(shape4)
    v4 = v3.reshape(shape4)
    inside = jnp.cumsum(g3.reshape(shape4), axis=1)
    span_total = inside[:, -1]
    span_end = jnp.cumsum(span_total, axis=0)
    span_start = span_end - span_total
    span_state = jnp.einsum(
        "cshk,cshv->chkv", k4 * jnp.exp(span_total[:, None] - inside), v4, precision=TOP
    )
    end_state = jnp.einsum(
        "chk,chkv->hkv", jnp.exp(span_end[-1][None] - span_end), span_state, precision=TOP
    )
    state_in = carried_in(jnp.exp(span_end[-1]), end_state, 2 * n_pairs)

    causal = (jnp.arange(SPAN)[:, None] >= jnp.arange(SPAN)[None, :])[None, :, :, None, None]
    gap_log = jnp.where(causal, inside[:, :, None] - inside[:, None, :], 0.0)
    decay_pairs = jnp.where(causal, jnp.exp(gap_log), 0.0)
    scores = jnp.einsum("ctnk,ctsnk->ctsn", q4, decay_pairs * k4[:, None], precision=TOP)
    intra = jnp.einsum("ctsn,csnv->ctnv", scores, v4, precision=TOP)
    earlier = (jnp.arange(spans)[:, None] > jnp.arange(spans)[None, :])[:, :, None, None]
    weights = jnp.where(
        earlier, jnp.exp(jnp.where(earlier, span_start[:, None] - span_end[None, :], 0.0)), 0.0
    )
    local_in = jnp.einsum("cdhk,dhkv->chkv", weights, span_state, precision=TOP)
    local_out = intra + jnp.einsum("cthk,chkv->cthv", q4 * jnp.exp(inside), local_in, precision=TOP)
    running = inside + span_start[:, None]
    heads_out = local_out + jnp.einsum("cthk,hkv->cthv", q4 * jnp.exp(running), state_in, precision=TOP)
    heads_out = heads_out.reshape(shape3)
    mean_sq = jnp.mean(heads_out * heads_out, axis=-1, keepdims=True)
    head_normed = (
        heads_out / jnp.sqrt(mean_sq + 1e-06) * head_gain.reshape(heads_here, HEAD)
    ).astype(jnp.bfloat16)
    head_normed = head_normed.reshape(slot_total, quarter)
    partial_rows = to_natural(lax.dot_general(
        head_normed, out_t, (((1,), (1,)), ((), ())), preferred_element_type=jnp.float32
    ).astype(jnp.bfloat16), n_pairs)
    mixed_cols = mlp_sum(partial_rows, n_mlp)
    my_cols = lax.axis_index("mlp") * quarter
    own_res = lax.dynamic_slice_in_dim(residual, my_cols, quarter, 1).astype(jnp.float32)
    stream_cols = (own_res + mixed_cols).astype(jnp.bfloat16)
    stream = mlp_gather(stream_cols, n_mlp)

    rows_f = stream.astype(jnp.float32)
    ffn_in = (
        rows_f / jnp.sqrt(jnp.mean(rows_f * rows_f, axis=-1, keepdims=True) + 1e-05) * ffn_gain
    ).astype(jnp.bfloat16)
    ffn_in = to_gathered(ffn_in, n_pairs)
    gate_acc = jnp.dot(ffn_in, gate_full, preferred_element_type=jnp.float32)
    up_acc = jnp.dot(ffn_in, up_full, preferred_element_type=jnp.float32)
    hidden = (jax.nn.silu(gate_acc) * up_acc).astype(jnp.bfloat16)
    terms = to_natural(lax.dot_general(
        hidden, down_t, (((1,), (1,)), ((), ())), preferred_element_type=jnp.float32
    ).astype(jnp.bfloat16), n_pairs)
    ffn_out = mlp_sum(terms, n_mlp)
    result = (stream_cols.astype(jnp.float32) + ffn_out).astype(jnp.bfloat16)
    return jnp.where(live_mask[:, None], result, jnp.zeros_like(result))


def solution(mesh):
    n_req = mesh.shape["req"]
    n_mlp = mesh.shape["mlp"]
    n_pairs = n_req // 2
    split = Mesh(mesh.devices.reshape(n_pairs, 2, n_mlp), ("rp", "rc", "mlp"))

    def body(*args):
        return on_device(*args, n_pairs=n_pairs, n_mlp=n_mlp)

    return jax.shard_map(
        body,
        mesh=split,
        in_specs=(
            P(REQ, None),
            P(REQ, "mlp"),
            P(REQ, "mlp"),
            P(REQ, "mlp"),
            P(REQ),
            P("mlp"),
            P("mlp", REQ),
            P(),
            P(REQ, "mlp"),
            P(REQ, "mlp"),
            P("mlp", REQ),
        ),
        out_specs=P(REQ, "mlp"),
        check_vma=False,
    )
```

```python
import jax
import jax.numpy as jnp
from jax import lax
from jax.sharding import Mesh, PartitionSpec as P

HEAD = 128
SPAN = 32
TOP = lax.Precision.HIGHEST
REQ = ("rp", "rc")


def compose(earlier, later):
    decay = later[:, HEAD:, :]
    joined = decay.transpose(0, 2, 1) * earlier[:, :HEAD, :] + later[:, :HEAD, :]
    return jnp.concatenate([joined, earlier[:, HEAD:, :] * decay], axis=1)


def carried_in(decay, state, count):
    place = lax.axis_index(REQ)
    packed = jnp.concatenate([state, decay[:, None, :]], axis=1)

    def shifted(buf, hop):
        return lax.ppermute(buf, REQ, [(i, i + hop) for i in range(count - hop)])

    reach = 1
    while 2 * reach < count:
        offsets = [j * reach for j in (1, 2, 3) if j * reach < count]
        got = [shifted(packed, hop) for hop in offsets]
        for hop, piece in zip(offsets, got):
            packed = jnp.where(place >= hop, compose(piece, packed), packed)
        reach *= 4
    last = shifted(packed, 1)
    if reach + 1 < count:
        far = shifted(packed, reach + 1)
        last = jnp.where(place >= reach + 1, compose(far, last), last)
    return last[:, :HEAD, :]


def mlp_sum(parts, n_mlp):
    rows, width = parts.shape
    blocks = parts.reshape(rows, n_mlp, width // n_mlp).transpose(1, 0, 2)
    got = lax.all_to_all(blocks, "mlp", 0, 0)
    return jnp.sum(got.astype(jnp.float32), axis=0)


def mlp_gather(cols, n_mlp):
    rows, width = cols.shape
    sent = jnp.broadcast_to(cols[None], (n_mlp, rows, width))
    got = lax.all_to_all(sent, "mlp", 0, 0)
    return got.transpose(1, 0, 2).reshape(rows, n_mlp * width)


def gather_rows(piece, n_pairs):
    over_chips = lax.all_gather(piece, "rp", axis=0)
    sent = jnp.broadcast_to(over_chips[None], (2,) + over_chips.shape)
    over_cores = lax.all_to_all(sent, "rc", 0, 0)
    return over_cores.reshape(2 * n_pairs * piece.shape[0], piece.shape[1])


def to_natural(cols, n_pairs):
    rows, width = cols.shape
    return cols.reshape(rows, 2, n_pairs, -1).transpose(0, 2, 1, 3).reshape(rows, width)


def to_gathered(cols, n_pairs):
    rows, width = cols.shape
    return cols.reshape(rows, n_pairs, 2, -1).transpose(0, 2, 1, 3).reshape(rows, width)


def on_device(
    residual,
    query_rows,
    value_rows,
    forget_logit,
    slot_kind,
    head_gain,
    out_weight,
    ffn_gain,
    gate_weight,
    up_weight,
    down_weight,
    *,
    n_pairs,
    n_mlp,
):
    slot_total = residual.shape[0]
    quarter = query_rows.shape[1]
    heads_here = quarter // HEAD
    hidden_here = gate_weight.shape[1]

    quarter_cols = 2 * hidden_here
    full = gather_rows(
        jnp.concatenate([gate_weight, up_weight, out_weight.T, down_weight.T], axis=1), n_pairs
    )
    gate_full = full[:, :hidden_here]
    up_full = full[:, hidden_here:quarter_cols]
    out_t = full[:, quarter_cols:quarter_cols + quarter]
    down_t = full[:, quarter_cols + quarter:]

    live_mask = slot_kind > 0
    first_mask = slot_kind == 2
    log_forget = jnp.where(
        first_mask[:, None],
        -80.0,
        jnp.where(live_mask[:, None], -jax.nn.softplus(-forget_logit), 0.0),
    )
    key_gate = jnp.where(live_mask[:, None], jax.nn.sigmoid(-forget_logit), 0.0)
    shape3 = (slot_total, heads_here, HEAD)
    q3 = query_rows.astype(jnp.float32).reshape(shape3)
    v3 = value_rows.astype(jnp.float32).reshape(shape3)
    k3 = key_gate.reshape(shape3)
    g3 = log_forget.reshape(shape3)

    spans = slot_total // SPAN
    shape4 = (spans, SPAN, heads_here, HEAD)
    q4 = q3.reshape(shape4)
    k4 = k3.reshape(shape4)
    v4 = v3.reshape(shape4)
    inside = jnp.cumsum(g3.reshape(shape4), axis=1)
    span_total = inside[:, -1]
    span_end = jnp.cumsum(span_total, axis=0)
    span_start = span_end - span_total
    span_state = jnp.einsum(
        "cshk,cshv->chkv", k4 * jnp.exp(span_total[:, None] - inside), v4, precision=TOP
    )
    end_state = jnp.einsum(
        "chk,chkv->hkv", jnp.exp(span_end[-1][None] - span_end), span_state, precision=TOP
    )
    state_in = carried_in(jnp.exp(span_end[-1]), end_state, 2 * n_pairs)

    causal = (jnp.arange(SPAN)[:, None] >= jnp.arange(SPAN)[None, :])[None, :, :, None, None]
    gap_log = jnp.where(causal, inside[:, :, None] - inside[:, None, :], 0.0)
    decay_pairs = jnp.where(causal, jnp.exp(gap_log), 0.0)
    scores = jnp.einsum("ctnk,ctsnk->ctsn", q4, decay_pairs * k4[:, None], precision=TOP)
    intra = jnp.einsum("ctsn,csnv->ctnv", scores, v4, precision=TOP)
    earlier = (jnp.arange(spans)[:, None] > jnp.arange(spans)[None, :])[:, :, None, None]
    weights = jnp.where(
        earlier, jnp.exp(jnp.where(earlier, span_start[:, None] - span_end[None, :], 0.0)), 0.0
    )
    local_in = jnp.einsum("cdhk,dhkv->chkv", weights, span_state, precision=TOP)
    local_out = intra + jnp.einsum("cthk,chkv->cthv", q4 * jnp.exp(inside), local_in, precision=TOP)
    running = inside + span_start[:, None]
    heads_out = local_out + jnp.einsum("cthk,hkv->cthv", q4 * jnp.exp(running), state_in, precision=TOP)
    heads_out = heads_out.reshape(shape3)
    mean_sq = jnp.mean(heads_out * heads_out, axis=-1, keepdims=True)
    head_normed = (
        heads_out / jnp.sqrt(mean_sq + 1e-06) * head_gain.reshape(heads_here, HEAD)
    ).astype(jnp.bfloat16)
    head_normed = head_normed.reshape(slot_total, quarter)
    partial_rows = to_natural(lax.dot_general(
        head_normed, out_t, (((1,), (1,)), ((), ())), preferred_element_type=jnp.float32
    ).astype(jnp.bfloat16), n_pairs)
    mixed_cols = mlp_sum(partial_rows, n_mlp)
    my_cols = lax.axis_index("mlp") * quarter
    own_res = lax.dynamic_slice_in_dim(residual, my_cols, quarter, 1).astype(jnp.float32)
    stream_cols = (own_res + mixed_cols).astype(jnp.bfloat16)
    stream = mlp_gather(stream_cols, n_mlp)

    rows_f = stream.astype(jnp.float32)
    ffn_in = (
        rows_f / jnp.sqrt(jnp.mean(rows_f * rows_f, axis=-1, keepdims=True) + 1e-05) * ffn_gain
    ).astype(jnp.bfloat16)
    ffn_in = to_gathered(ffn_in, n_pairs)
    gate_acc = jnp.dot(ffn_in, gate_full, preferred_element_type=jnp.float32)
    up_acc = jnp.dot(ffn_in, up_full, preferred_element_type=jnp.float32)
    hidden = (jax.nn.silu(gate_acc) * up_acc).astype(jnp.bfloat16)
    terms = to_natural(lax.dot_general(
        hidden, down_t, (((1,), (1,)), ((), ())), preferred_element_type=jnp.float32
    ).astype(jnp.bfloat16), n_pairs)
    ffn_out = mlp_sum(terms, n_mlp)
    result = (stream_cols.astype(jnp.float32) + ffn_out).astype(jnp.bfloat16)
    return jnp.where(live_mask[:, None], result, jnp.zeros_like(result))


def solution(mesh):
    n_req = mesh.shape["req"]
    n_mlp = mesh.shape["mlp"]
    n_pairs = n_req // 2
    split = Mesh(mesh.devices.reshape(n_pairs, 2, n_mlp), ("rp", "rc", "mlp"))

    def body(*args):
        return on_device(*args, n_pairs=n_pairs, n_mlp=n_mlp)

    return jax.shard_map(
        body,
        mesh=split,
        in_specs=(
            P(REQ, None),
            P(REQ, "mlp"),
            P(REQ, "mlp"),
            P(REQ, "mlp"),
            P(REQ),
            P("mlp"),
            P("mlp", REQ),
            P(),
            P(REQ, "mlp"),
            P(REQ, "mlp"),
            P("mlp", REQ),
        ),
        out_specs=P(REQ, "mlp"),
        check_vma=False,
    )
```

```python
import jax
import jax.numpy as jnp
from jax import lax
from jax.sharding import Mesh, PartitionSpec as P

HEAD = 128
SPAN = 32
TOP = lax.Precision.HIGHEST
REQ = ("rp", "rc")


def compose(earlier, later):
    decay = later[:, HEAD:, :]
    joined = decay.transpose(0, 2, 1) * earlier[:, :HEAD, :] + later[:, :HEAD, :]
    return jnp.concatenate([joined, earlier[:, HEAD:, :] * decay], axis=1)


def carried_in(decay, state, count):
    place = lax.axis_index(REQ)
    packed = jnp.concatenate([state, decay[:, None, :]], axis=1)
    hop = 1
    while hop < count:
        got = lax.ppermute(packed, REQ, [(i, i + hop) for i in range(count - hop)])
        packed = jnp.where(place >= hop, compose(got, packed), packed)
        hop *= 2
    shifted = lax.ppermute(packed, REQ, [(i, i + 1) for i in range(count - 1)])
    return shifted[:, :HEAD, :]


def mlp_sum(parts, n_mlp):
    rows, width = parts.shape
    blocks = parts.reshape(rows, n_mlp, width // n_mlp).transpose(1, 0, 2)
    got = lax.all_to_all(blocks, "mlp", 0, 0)
    return jnp.sum(got.astype(jnp.float32), axis=0)


def gather_rows(piece, n_pairs):
    over_chips = lax.all_gather(piece, "rp", axis=0)
    sent = jnp.broadcast_to(over_chips[None], (2,) + over_chips.shape)
    over_cores = lax.all_to_all(sent, "rc", 0, 0)
    return over_cores.reshape(2 * n_pairs * piece.shape[0], piece.shape[1])


def to_natural(cols, n_pairs):
    rows, width = cols.shape
    return cols.reshape(rows, 2, n_pairs, -1).transpose(0, 2, 1, 3).reshape(rows, width)


def to_gathered(cols, n_pairs):
    rows, width = cols.shape
    return cols.reshape(rows, n_pairs, 2, -1).transpose(0, 2, 1, 3).reshape(rows, width)


def on_device(
    residual,
    query_rows,
    value_rows,
    forget_logit,
    slot_kind,
    head_gain,
    out_weight,
    ffn_gain,
    gate_weight,
    up_weight,
    down_weight,
    *,
    n_pairs,
    n_mlp,
):
    slot_total = residual.shape[0]
    quarter = query_rows.shape[1]
    heads_here = quarter // HEAD
    hidden_here = gate_weight.shape[1]

    quarter_cols = 2 * hidden_here
    full = gather_rows(
        jnp.concatenate([gate_weight, up_weight, out_weight.T, down_weight.T], axis=1), n_pairs
    )
    gate_full = full[:, :hidden_here]
    up_full = full[:, hidden_here:quarter_cols]
    out_t = full[:, quarter_cols:quarter_cols + quarter]
    down_t = full[:, quarter_cols + quarter:]

    live_mask = slot_kind > 0
    first_mask = slot_kind == 2
    log_forget = jnp.where(
        first_mask[:, None],
        -80.0,
        jnp.where(live_mask[:, None], -jax.nn.softplus(-forget_logit), 0.0),
    )
    key_gate = jnp.where(live_mask[:, None], jax.nn.sigmoid(-forget_logit), 0.0)
    shape3 = (slot_total, heads_here, HEAD)
    q3 = query_rows.astype(jnp.float32).reshape(shape3)
    v3 = value_rows.astype(jnp.float32).reshape(shape3)
    k3 = key_gate.reshape(shape3)
    g3 = log_forget.reshape(shape3)

    spans = slot_total // SPAN
    shape4 = (spans, SPAN, heads_here, HEAD)
    q4 = q3.reshape(shape4)
    k4 = k3.reshape(shape4)
    v4 = v3.reshape(shape4)
    inside = jnp.cumsum(g3.reshape(shape4), axis=1)
    span_total = inside[:, -1]
    span_end = jnp.cumsum(span_total, axis=0)
    span_start = span_end - span_total
    span_state = jnp.einsum(
        "cshk,cshv->chkv", k4 * jnp.exp(span_total[:, None] - inside), v4, precision=TOP
    )
    end_state = jnp.einsum(
        "chk,chkv->hkv", jnp.exp(span_end[-1][None] - span_end), span_state, precision=TOP
    )
    state_in = carried_in(jnp.exp(span_end[-1]), end_state, 2 * n_pairs)

    causal = (jnp.arange(SPAN)[:, None] >= jnp.arange(SPAN)[None, :])[None, :, :, None, None]
    gap_log = jnp.where(causal, inside[:, :, None] - inside[:, None, :], 0.0)
    decay_pairs = jnp.where(causal, jnp.exp(gap_log), 0.0)
    scores = jnp.einsum("ctnk,ctsnk->ctsn", q4, decay_pairs * k4[:, None], precision=TOP)
    intra = jnp.einsum("ctsn,csnv->ctnv", scores, v4, precision=TOP)
    earlier = (jnp.arange(spans)[:, None] > jnp.arange(spans)[None, :])[:, :, None, None]
    weights = jnp.where(
        earlier, jnp.exp(jnp.where(earlier, span_start[:, None] - span_end[None, :], 0.0)), 0.0
    )
    local_in = jnp.einsum("cdhk,dhkv->chkv", weights, span_state, precision=TOP)
    local_out = intra + jnp.einsum("cthk,chkv->cthv", q4 * jnp.exp(inside), local_in, precision=TOP)
    running = inside + span_start[:, None]
    heads_out = local_out + jnp.einsum("cthk,hkv->cthv", q4 * jnp.exp(running), state_in, precision=TOP)
    heads_out = heads_out.reshape(shape3)
    mean_sq = jnp.mean(heads_out * heads_out, axis=-1, keepdims=True)
    head_normed = (
        heads_out / jnp.sqrt(mean_sq + 1e-06) * head_gain.reshape(heads_here, HEAD)
    ).astype(jnp.bfloat16)
    head_normed = head_normed.reshape(slot_total, quarter)
    partial_rows = to_natural(lax.dot_general(
        head_normed, out_t, (((1,), (1,)), ((), ())), preferred_element_type=jnp.float32
    ).astype(jnp.bfloat16), n_pairs)
    every = lax.all_to_all(
        jnp.broadcast_to(partial_rows[None], (n_mlp,) + partial_rows.shape), "mlp", 0, 0
    )
    mixed = jnp.sum(every.astype(jnp.float32), axis=0)
    stream = (residual.astype(jnp.float32) + mixed).astype(jnp.bfloat16)
    my_cols = lax.axis_index("mlp") * quarter
    stream_cols = lax.dynamic_slice_in_dim(stream, my_cols, quarter, 1)

    rows_f = stream.astype(jnp.float32)
    ffn_in = (
        rows_f / jnp.sqrt(jnp.mean(rows_f * rows_f, axis=-1, keepdims=True) + 1e-05) * ffn_gain
    ).astype(jnp.bfloat16)
    ffn_in = to_gathered(ffn_in, n_pairs)
    gate_acc = jnp.dot(ffn_in, gate_full, preferred_element_type=jnp.float32)
    up_acc = jnp.dot(ffn_in, up_full, preferred_element_type=jnp.float32)
    hidden = (jax.nn.silu(gate_acc) * up_acc).astype(jnp.bfloat16)
    terms = to_natural(lax.dot_general(
        hidden, down_t, (((1,), (1,)), ((), ())), preferred_element_type=jnp.float32
    ).astype(jnp.bfloat16), n_pairs)
    ffn_out = mlp_sum(terms, n_mlp)
    result = (stream_cols.astype(jnp.float32) + ffn_out).astype(jnp.bfloat16)
    return jnp.where(live_mask[:, None], result, jnp.zeros_like(result))


def solution(mesh):
    n_req = mesh.shape["req"]
    n_mlp = mesh.shape["mlp"]
    n_pairs = n_req // 2
    split = Mesh(mesh.devices.reshape(n_pairs, 2, n_mlp), ("rp", "rc", "mlp"))

    def body(*args):
        return on_device(*args, n_pairs=n_pairs, n_mlp=n_mlp)

    return jax.shard_map(
        body,
        mesh=split,
        in_specs=(
            P(REQ, None),
            P(REQ, "mlp"),
            P(REQ, "mlp"),
            P(REQ, "mlp"),
            P(REQ),
            P("mlp"),
            P("mlp", REQ),
            P(),
            P(REQ, "mlp"),
            P(REQ, "mlp"),
            P("mlp", REQ),
        ),
        out_specs=P(REQ, "mlp"),
        check_vma=False,
    )
```

```python
import jax
import jax.numpy as jnp
from jax import lax
from jax.sharding import Mesh, PartitionSpec as P

HEAD = 128
SPAN = 32
TOP = lax.Precision.HIGHEST
REQ = ("rp", "rc")


def compose(earlier, later):
    decay = later[:, HEAD:, :]
    joined = decay.transpose(0, 2, 1) * earlier[:, :HEAD, :] + later[:, :HEAD, :]
    return jnp.concatenate([joined, earlier[:, HEAD:, :] * decay], axis=1)


def carried_in(decay, state, count):
    place = lax.axis_index(REQ)
    packed = jnp.concatenate([state, decay[:, None, :]], axis=1)
    hop = 1
    while hop < count:
        got = lax.ppermute(packed, REQ, [(i, i + hop) for i in range(count - hop)])
        packed = jnp.where(place >= hop, compose(got, packed), packed)
        hop *= 2
    shifted = lax.ppermute(packed, REQ, [(i, i + 1) for i in range(count - 1)])
    return shifted[:, :HEAD, :]


def mlp_sum(parts, n_mlp):
    rows, width = parts.shape
    blocks = parts.reshape(rows, n_mlp, width // n_mlp).transpose(1, 0, 2)
    got = lax.all_to_all(blocks, "mlp", 0, 0)
    return jnp.sum(got.astype(jnp.float32), axis=0)


def mlp_gather(cols, n_mlp):
    rows, width = cols.shape
    sent = jnp.broadcast_to(cols[None], (n_mlp, rows, width))
    got = lax.all_to_all(sent, "mlp", 0, 0)
    return got.transpose(1, 0, 2).reshape(rows, n_mlp * width)


def join_cores(parts, core, n_pairs):
    own, partner = (p.reshape(p.shape[0], n_pairs, 1, -1) for p in parts)
    both = jnp.where(core == 0, jnp.concatenate([own, partner], 2), jnp.concatenate([partner, own], 2))
    return both.reshape(both.shape[0], -1)


def split_cores(cols, core, n_pairs):
    rows = cols.shape[0]
    four = cols.reshape(rows, n_pairs, 2, -1)
    own = lax.dynamic_index_in_dim(four, core, 2, False)
    partner = lax.dynamic_index_in_dim(four, 1 - core, 2, False)
    return own.reshape(rows, -1), partner.reshape(rows, -1)


def on_device(
    residual,
    query_rows,
    value_rows,
    forget_logit,
    slot_kind,
    head_gain,
    out_weight,
    ffn_gain,
    gate_weight,
    up_weight,
    down_weight,
    *,
    n_pairs,
    n_mlp,
):
    slot_total = residual.shape[0]
    quarter = query_rows.shape[1]
    heads_here = quarter // HEAD
    hidden_here = gate_weight.shape[1]

    quarter_cols = 2 * hidden_here
    mine = lax.all_gather(
        jnp.concatenate([gate_weight, up_weight, out_weight.T, down_weight.T], axis=1), "rp", axis=0
    )
    mine = mine.reshape(-1, mine.shape[-1])
    other = lax.ppermute(mine, "rc", [(0, 1), (1, 0)])
    core = lax.axis_index("rc")
    halves = (mine, other)

    live_mask = slot_kind > 0
    first_mask = slot_kind == 2
    log_forget = jnp.where(
        first_mask[:, None],
        -80.0,
        jnp.where(live_mask[:, None], -jax.nn.softplus(-forget_logit), 0.0),
    )
    key_gate = jnp.where(live_mask[:, None], jax.nn.sigmoid(-forget_logit), 0.0)
    shape3 = (slot_total, heads_here, HEAD)
    q3 = query_rows.astype(jnp.float32).reshape(shape3)
    v3 = value_rows.astype(jnp.float32).reshape(shape3)
    k3 = key_gate.reshape(shape3)
    g3 = log_forget.reshape(shape3)

    spans = slot_total // SPAN
    shape4 = (spans, SPAN, heads_here, HEAD)
    q4 = q3.reshape(shape4)
    k4 = k3.reshape(shape4)
    v4 = v3.reshape(shape4)
    inside = jnp.cumsum(g3.reshape(shape4), axis=1)
    span_total = inside[:, -1]
    span_end = jnp.cumsum(span_total, axis=0)
    span_start = span_end - span_total
    span_state = jnp.einsum(
        "cshk,cshv->chkv", k4 * jnp.exp(span_total[:, None] - inside), v4, precision=TOP
    )
    end_state = jnp.einsum(
        "chk,chkv->hkv", jnp.exp(span_end[-1][None] - span_end), span_state, precision=TOP
    )
    state_in = carried_in(jnp.exp(span_end[-1]), end_state, 2 * n_pairs)

    causal = (jnp.arange(SPAN)[:, None] >= jnp.arange(SPAN)[None, :])[None, :, :, None, None]
    gap_log = jnp.where(causal, inside[:, :, None] - inside[:, None, :], 0.0)
    decay_pairs = jnp.where(causal, jnp.exp(gap_log), 0.0)
    scores = jnp.einsum("ctnk,ctsnk->ctsn", q4, decay_pairs * k4[:, None], precision=TOP)
    intra = jnp.einsum("ctsn,csnv->ctnv", scores, v4, precision=TOP)
    earlier = (jnp.arange(spans)[:, None] > jnp.arange(spans)[None, :])[:, :, None, None]
    weights = jnp.where(
        earlier, jnp.exp(jnp.where(earlier, span_start[:, None] - span_end[None, :], 0.0)), 0.0
    )
    local_in = jnp.einsum("cdhk,dhkv->chkv", weights, span_state, precision=TOP)
    local_out = intra + jnp.einsum("cthk,chkv->cthv", q4 * jnp.exp(inside), local_in, precision=TOP)
    running = inside + span_start[:, None]
    heads_out = local_out + jnp.einsum("cthk,hkv->cthv", q4 * jnp.exp(running), state_in, precision=TOP)
    heads_out = heads_out.reshape(shape3)
    mean_sq = jnp.mean(heads_out * heads_out, axis=-1, keepdims=True)
    head_normed = (
        heads_out / jnp.sqrt(mean_sq + 1e-06) * head_gain.reshape(heads_here, HEAD)
    ).astype(jnp.bfloat16)
    head_normed = head_normed.reshape(slot_total, quarter)
    partial_rows = join_cores(
        [
            lax.dot_general(
                head_normed, half[:, quarter_cols:quarter_cols + quarter], (((1,), (1,)), ((), ())),
                preferred_element_type=jnp.float32,
            ).astype(jnp.bfloat16)
            for half in halves
        ],
        core, n_pairs,
    )
    mixed_cols = mlp_sum(partial_rows, n_mlp)
    my_cols = lax.axis_index("mlp") * quarter
    own_res = lax.dynamic_slice_in_dim(residual, my_cols, quarter, 1).astype(jnp.float32)
    stream_cols = (own_res + mixed_cols).astype(jnp.bfloat16)
    stream = mlp_gather(stream_cols, n_mlp)

    rows_f = stream.astype(jnp.float32)
    ffn_in = (
        rows_f / jnp.sqrt(jnp.mean(rows_f * rows_f, axis=-1, keepdims=True) + 1e-05) * ffn_gain
    ).astype(jnp.bfloat16)
    split_in = split_cores(ffn_in, core, n_pairs)
    gate_acc = sum(
        jnp.dot(part, half[:, :hidden_here], preferred_element_type=jnp.float32)
        for part, half in zip(split_in, halves)
    )
    up_acc = sum(
        jnp.dot(part, half[:, hidden_here:quarter_cols], preferred_element_type=jnp.float32)
        for part, half in zip(split_in, halves)
    )
    hidden = (jax.nn.silu(gate_acc) * up_acc).astype(jnp.bfloat16)
    terms = join_cores(
        [
            lax.dot_general(
                hidden, half[:, quarter_cols + quarter:], (((1,), (1,)), ((), ())),
                preferred_element_type=jnp.float32,
            ).astype(jnp.bfloat16)
            for half in halves
        ],
        core, n_pairs,
    )
    ffn_out = mlp_sum(terms, n_mlp)
    result = (stream_cols.astype(jnp.float32) + ffn_out).astype(jnp.bfloat16)
    return jnp.where(live_mask[:, None], result, jnp.zeros_like(result))


def solution(mesh):
    n_req = mesh.shape["req"]
    n_mlp = mesh.shape["mlp"]
    n_pairs = n_req // 2
    split = Mesh(mesh.devices.reshape(n_pairs, 2, n_mlp), ("rp", "rc", "mlp"))

    def body(*args):
        return on_device(*args, n_pairs=n_pairs, n_mlp=n_mlp)

    return jax.shard_map(
        body,
        mesh=split,
        in_specs=(
            P(REQ, None),
            P(REQ, "mlp"),
            P(REQ, "mlp"),
            P(REQ, "mlp"),
            P(REQ),
            P("mlp"),
            P("mlp", REQ),
            P(),
            P(REQ, "mlp"),
            P(REQ, "mlp"),
            P("mlp", REQ),
        ),
        out_specs=P(REQ, "mlp"),
        check_vma=False,
    )
```

```python
import jax
import jax.numpy as jnp
from jax import lax
from jax.sharding import Mesh, PartitionSpec as P

HEAD = 128
SPAN = 32
TOP = lax.Precision.HIGHEST
REQ = ("rp", "rc")


def compose(earlier, later):
    decay = later[:, HEAD:, :]
    joined = decay.transpose(0, 2, 1) * earlier[:, :HEAD, :] + later[:, :HEAD, :]
    return jnp.concatenate([joined, earlier[:, HEAD:, :] * decay], axis=1)


def carried_in(decay, state, count):
    place = lax.axis_index(REQ)
    packed = jnp.concatenate([state, decay[:, None, :]], axis=1)
    hop = 1
    while hop < count:
        got = lax.ppermute(packed, REQ, [(i, i + hop) for i in range(count - hop)])
        packed = jnp.where(place >= hop, compose(got, packed), packed)
        hop *= 2
    shifted = lax.ppermute(packed, REQ, [(i, i + 1) for i in range(count - 1)])
    return shifted[:, :HEAD, :]


def mlp_sum(parts, n_mlp):
    rows, width = parts.shape
    blocks = parts.reshape(rows, n_mlp, width // n_mlp).transpose(1, 0, 2)
    got = lax.all_to_all(blocks, "mlp", 0, 0)
    return jnp.sum(got.astype(jnp.float32), axis=0)


def mlp_gather(cols, n_mlp):
    rows, width = cols.shape
    sent = jnp.broadcast_to(cols[None], (n_mlp, rows, width))
    got = lax.all_to_all(sent, "mlp", 0, 0)
    return got.transpose(1, 0, 2).reshape(rows, n_mlp * width)


def join_cores(parts, core, n_pairs):
    own, partner = (p.reshape(p.shape[0], n_pairs, 1, -1) for p in parts)
    both = jnp.where(core == 0, jnp.concatenate([own, partner], 2), jnp.concatenate([partner, own], 2))
    return both.reshape(both.shape[0], -1)


def split_cores(cols, core, n_pairs):
    rows = cols.shape[0]
    four = cols.reshape(rows, n_pairs, 2, -1)
    own = lax.dynamic_index_in_dim(four, core, 2, False)
    partner = lax.dynamic_index_in_dim(four, 1 - core, 2, False)
    return own.reshape(rows, -1), partner.reshape(rows, -1)


def on_device(
    residual,
    query_rows,
    value_rows,
    forget_logit,
    slot_kind,
    head_gain,
    out_weight,
    ffn_gain,
    gate_weight,
    up_weight,
    down_weight,
    *,
    n_pairs,
    n_mlp,
):
    slot_total = residual.shape[0]
    quarter = query_rows.shape[1]
    heads_here = quarter // HEAD
    hidden_here = gate_weight.shape[1]

    quarter_cols = 2 * hidden_here
    mine = lax.all_gather(
        jnp.concatenate([gate_weight, up_weight, out_weight.T, down_weight.T], axis=1), "rp", axis=0
    )
    mine = mine.reshape(-1, mine.shape[-1])
    core = lax.axis_index("rc")

    live_mask = slot_kind > 0
    first_mask = slot_kind == 2
    log_forget = jnp.where(
        first_mask[:, None],
        -80.0,
        jnp.where(live_mask[:, None], -jax.nn.softplus(-forget_logit), 0.0),
    )
    key_gate = jnp.where(live_mask[:, None], jax.nn.sigmoid(-forget_logit), 0.0)
    shape3 = (slot_total, heads_here, HEAD)
    q3 = query_rows.astype(jnp.float32).reshape(shape3)
    v3 = value_rows.astype(jnp.float32).reshape(shape3)
    k3 = key_gate.reshape(shape3)
    g3 = log_forget.reshape(shape3)

    spans = slot_total // SPAN
    shape4 = (spans, SPAN, heads_here, HEAD)
    q4 = q3.reshape(shape4)
    k4 = k3.reshape(shape4)
    v4 = v3.reshape(shape4)
    inside = jnp.cumsum(g3.reshape(shape4), axis=1)
    span_total = inside[:, -1]
    span_end = jnp.cumsum(span_total, axis=0)
    span_start = span_end - span_total
    span_state = jnp.einsum(
        "cshk,cshv->chkv", k4 * jnp.exp(span_total[:, None] - inside), v4, precision=TOP
    )
    end_state = jnp.einsum(
        "chk,chkv->hkv", jnp.exp(span_end[-1][None] - span_end), span_state, precision=TOP
    )
    state_in = carried_in(jnp.exp(span_end[-1]), end_state, 2 * n_pairs)
    mine, state_in = lax.optimization_barrier((mine, state_in))
    halves = (mine, lax.ppermute(mine, "rc", [(0, 1), (1, 0)]))

    causal = (jnp.arange(SPAN)[:, None] >= jnp.arange(SPAN)[None, :])[None, :, :, None, None]
    gap_log = jnp.where(causal, inside[:, :, None] - inside[:, None, :], 0.0)
    decay_pairs = jnp.where(causal, jnp.exp(gap_log), 0.0)
    scores = jnp.einsum("ctnk,ctsnk->ctsn", q4, decay_pairs * k4[:, None], precision=TOP)
    intra = jnp.einsum("ctsn,csnv->ctnv", scores, v4, precision=TOP)
    earlier = (jnp.arange(spans)[:, None] > jnp.arange(spans)[None, :])[:, :, None, None]
    weights = jnp.where(
        earlier, jnp.exp(jnp.where(earlier, span_start[:, None] - span_end[None, :], 0.0)), 0.0
    )
    local_in = jnp.einsum("cdhk,dhkv->chkv", weights, span_state, precision=TOP)
    local_out = intra + jnp.einsum("cthk,chkv->cthv", q4 * jnp.exp(inside), local_in, precision=TOP)
    running = inside + span_start[:, None]
    heads_out = local_out + jnp.einsum("cthk,hkv->cthv", q4 * jnp.exp(running), state_in, precision=TOP)
    heads_out = heads_out.reshape(shape3)
    mean_sq = jnp.mean(heads_out * heads_out, axis=-1, keepdims=True)
    head_normed = (
        heads_out / jnp.sqrt(mean_sq + 1e-06) * head_gain.reshape(heads_here, HEAD)
    ).astype(jnp.bfloat16)
    head_normed = head_normed.reshape(slot_total, quarter)
    partial_rows = join_cores(
        [
            lax.dot_general(
                head_normed, half[:, quarter_cols:quarter_cols + quarter], (((1,), (1,)), ((), ())),
                preferred_element_type=jnp.float32,
            ).astype(jnp.bfloat16)
            for half in halves
        ],
        core, n_pairs,
    )
    mixed_cols = mlp_sum(partial_rows, n_mlp)
    my_cols = lax.axis_index("mlp") * quarter
    own_res = lax.dynamic_slice_in_dim(residual, my_cols, quarter, 1).astype(jnp.float32)
    stream_cols = (own_res + mixed_cols).astype(jnp.bfloat16)
    stream = mlp_gather(stream_cols, n_mlp)

    rows_f = stream.astype(jnp.float32)
    ffn_in = (
        rows_f / jnp.sqrt(jnp.mean(rows_f * rows_f, axis=-1, keepdims=True) + 1e-05) * ffn_gain
    ).astype(jnp.bfloat16)
    split_in = split_cores(ffn_in, core, n_pairs)
    gate_acc = sum(
        jnp.dot(part, half[:, :hidden_here], preferred_element_type=jnp.float32)
        for part, half in zip(split_in, halves)
    )
    up_acc = sum(
        jnp.dot(part, half[:, hidden_here:quarter_cols], preferred_element_type=jnp.float32)
        for part, half in zip(split_in, halves)
    )
    hidden = (jax.nn.silu(gate_acc) * up_acc).astype(jnp.bfloat16)
    terms = join_cores(
        [
            lax.dot_general(
                hidden, half[:, quarter_cols + quarter:], (((1,), (1,)), ((), ())),
                preferred_element_type=jnp.float32,
            ).astype(jnp.bfloat16)
            for half in halves
        ],
        core, n_pairs,
    )
    ffn_out = mlp_sum(terms, n_mlp)
    result = (stream_cols.astype(jnp.float32) + ffn_out).astype(jnp.bfloat16)
    return jnp.where(live_mask[:, None], result, jnp.zeros_like(result))


def solution(mesh):
    n_req = mesh.shape["req"]
    n_mlp = mesh.shape["mlp"]
    n_pairs = n_req // 2
    split = Mesh(mesh.devices.reshape(n_pairs, 2, n_mlp), ("rp", "rc", "mlp"))

    def body(*args):
        return on_device(*args, n_pairs=n_pairs, n_mlp=n_mlp)

    return jax.shard_map(
        body,
        mesh=split,
        in_specs=(
            P(REQ, None),
            P(REQ, "mlp"),
            P(REQ, "mlp"),
            P(REQ, "mlp"),
            P(REQ),
            P("mlp"),
            P("mlp", REQ),
            P(),
            P(REQ, "mlp"),
            P(REQ, "mlp"),
            P("mlp", REQ),
        ),
        out_specs=P(REQ, "mlp"),
        check_vma=False,
    )
```

```python
import jax
import jax.numpy as jnp
from jax import lax
from jax.sharding import Mesh, PartitionSpec as P

HEAD = 128
SPAN = 32
TOP = lax.Precision.HIGHEST
REQ = ("rp", "rc")


def compose(earlier, later):
    decay = later[:, HEAD:, :]
    joined = decay.transpose(0, 2, 1) * earlier[:, :HEAD, :] + later[:, :HEAD, :]
    return jnp.concatenate([joined, earlier[:, HEAD:, :] * decay], axis=1)


def carried_in(decay, state, count):
    place = lax.axis_index(REQ)
    packed = jnp.concatenate([state, decay[:, None, :]], axis=1)
    def shifted(buf, hop):
        return lax.ppermute(buf, REQ, [(i, i + hop) for i in range(count - hop)])

    reach = 1
    while 2 * reach < count:
        packed = jnp.where(place >= reach, compose(shifted(packed, reach), packed), packed)
        reach *= 2
    last = shifted(packed, 1)
    if reach + 1 < count:
        far = shifted(packed, reach + 1)
        last = jnp.where(place >= reach + 1, compose(far, last), last)
    return last[:, :HEAD, :]


def mlp_sum(parts, n_mlp):
    rows, width = parts.shape
    blocks = parts.reshape(rows, n_mlp, width // n_mlp).transpose(1, 0, 2)
    got = lax.all_to_all(blocks, "mlp", 0, 0)
    return jnp.sum(got.astype(jnp.float32), axis=0)


def mlp_gather(cols, n_mlp):
    rows, width = cols.shape
    sent = jnp.broadcast_to(cols[None], (n_mlp, rows, width))
    got = lax.all_to_all(sent, "mlp", 0, 0)
    return got.transpose(1, 0, 2).reshape(rows, n_mlp * width)


def gather_rows(piece, n_pairs):
    over_chips = lax.all_gather(piece, "rp", axis=0)
    sent = jnp.broadcast_to(over_chips[None], (2,) + over_chips.shape)
    over_cores = lax.all_to_all(sent, "rc", 0, 0)
    return over_cores.reshape(2 * n_pairs * piece.shape[0], piece.shape[1])


def to_natural(cols, n_pairs):
    rows, width = cols.shape
    return cols.reshape(rows, 2, n_pairs, -1).transpose(0, 2, 1, 3).reshape(rows, width)


def to_gathered(cols, n_pairs):
    rows, width = cols.shape
    return cols.reshape(rows, n_pairs, 2, -1).transpose(0, 2, 1, 3).reshape(rows, width)


def on_device(
    residual,
    query_rows,
    value_rows,
    forget_logit,
    slot_kind,
    head_gain,
    out_weight,
    ffn_gain,
    gate_weight,
    up_weight,
    down_weight,
    *,
    n_pairs,
    n_mlp,
):
    slot_total = residual.shape[0]
    quarter = query_rows.shape[1]
    heads_here = quarter // HEAD
    hidden_here = gate_weight.shape[1]

    quarter_cols = 2 * hidden_here
    full = gather_rows(
        jnp.concatenate([gate_weight, up_weight, out_weight.T, down_weight.T], axis=1), n_pairs
    )
    gate_full = full[:, :hidden_here]
    up_full = full[:, hidden_here:quarter_cols]
    out_t = full[:, quarter_cols:quarter_cols + quarter]
    down_t = full[:, quarter_cols + quarter:]

    live_mask = slot_kind > 0
    first_mask = slot_kind == 2
    log_forget = jnp.where(
        first_mask[:, None],
        -80.0,
        jnp.where(live_mask[:, None], -jax.nn.softplus(-forget_logit), 0.0),
    )
    key_gate = jnp.where(live_mask[:, None], jax.nn.sigmoid(-forget_logit), 0.0)
    shape3 = (slot_total, heads_here, HEAD)
    q3 = query_rows.astype(jnp.float32).reshape(shape3)
    v3 = value_rows.astype(jnp.float32).reshape(shape3)
    k3 = key_gate.reshape(shape3)
    g3 = log_forget.reshape(shape3)

    spans = slot_total // SPAN
    shape4 = (spans, SPAN, heads_here, HEAD)
    q4 = q3.reshape(shape4)
    k4 = k3.reshape(shape4)
    v4 = v3.reshape(shape4)
    inside = jnp.cumsum(g3.reshape(shape4), axis=1)
    span_total = inside[:, -1]
    span_end = jnp.cumsum(span_total, axis=0)
    span_start = span_end - span_total
    span_state = jnp.einsum(
        "cshk,cshv->chkv", k4 * jnp.exp(span_total[:, None] - inside), v4, precision=TOP
    )
    end_state = jnp.einsum(
        "chk,chkv->hkv", jnp.exp(span_end[-1][None] - span_end), span_state, precision=TOP
    )
    state_in = carried_in(jnp.exp(span_end[-1]), end_state, 2 * n_pairs)

    causal = (jnp.arange(SPAN)[:, None] >= jnp.arange(SPAN)[None, :])[None, :, :, None, None]
    gap_log = jnp.where(causal, inside[:, :, None] - inside[:, None, :], 0.0)
    decay_pairs = jnp.where(causal, jnp.exp(gap_log), 0.0)
    scores = jnp.einsum("ctnk,ctsnk->ctsn", q4, decay_pairs * k4[:, None], precision=TOP)
    intra = jnp.einsum("ctsn,csnv->ctnv", scores, v4, precision=TOP)
    earlier = (jnp.arange(spans)[:, None] > jnp.arange(spans)[None, :])[:, :, None, None]
    weights = jnp.where(
        earlier, jnp.exp(jnp.where(earlier, span_start[:, None] - span_end[None, :], 0.0)), 0.0
    )
    local_in = jnp.einsum("cdhk,dhkv->chkv", weights, span_state, precision=TOP)
    local_out = intra + jnp.einsum("cthk,chkv->cthv", q4 * jnp.exp(inside), local_in, precision=TOP)
    running = inside + span_start[:, None]
    heads_out = local_out + jnp.einsum("cthk,hkv->cthv", q4 * jnp.exp(running), state_in, precision=TOP)
    heads_out = heads_out.reshape(shape3)
    mean_sq = jnp.mean(heads_out * heads_out, axis=-1, keepdims=True)
    head_normed = (
        heads_out / jnp.sqrt(mean_sq + 1e-06) * head_gain.reshape(heads_here, HEAD)
    ).astype(jnp.bfloat16)
    head_normed = head_normed.reshape(slot_total, quarter)
    partial_rows = to_natural(lax.dot_general(
        head_normed, out_t, (((1,), (1,)), ((), ())), preferred_element_type=jnp.float32
    ).astype(jnp.bfloat16), n_pairs)
    mixed_cols = mlp_sum(partial_rows, n_mlp)
    my_cols = lax.axis_index("mlp") * quarter
    own_res = lax.dynamic_slice_in_dim(residual, my_cols, quarter, 1).astype(jnp.float32)
    stream_cols = (own_res + mixed_cols).astype(jnp.bfloat16)
    stream = mlp_gather(stream_cols, n_mlp)

    rows_f = stream.astype(jnp.float32)
    ffn_in = (
        rows_f / jnp.sqrt(jnp.mean(rows_f * rows_f, axis=-1, keepdims=True) + 1e-05) * ffn_gain
    ).astype(jnp.bfloat16)
    ffn_in = to_gathered(ffn_in, n_pairs)
    gate_acc = jnp.dot(ffn_in, gate_full, preferred_element_type=jnp.float32)
    up_acc = jnp.dot(ffn_in, up_full, preferred_element_type=jnp.float32)
    hidden = (jax.nn.silu(gate_acc) * up_acc).astype(jnp.bfloat16)
    terms = to_natural(lax.dot_general(
        hidden, down_t, (((1,), (1,)), ((), ())), preferred_element_type=jnp.float32
    ).astype(jnp.bfloat16), n_pairs)
    ffn_out = mlp_sum(terms, n_mlp)
    result = (stream_cols.astype(jnp.float32) + ffn_out).astype(jnp.bfloat16)
    return jnp.where(live_mask[:, None], result, jnp.zeros_like(result))


def solution(mesh):
    n_req = mesh.shape["req"]
    n_mlp = mesh.shape["mlp"]
    n_pairs = n_req // 2
    split = Mesh(mesh.devices.reshape(n_pairs, 2, n_mlp), ("rp", "rc", "mlp"))

    def body(*args):
        return on_device(*args, n_pairs=n_pairs, n_mlp=n_mlp)

    return jax.shard_map(
        body,
        mesh=split,
        in_specs=(
            P(REQ, None),
            P(REQ, "mlp"),
            P(REQ, "mlp"),
            P(REQ, "mlp"),
            P(REQ),
            P("mlp"),
            P("mlp", REQ),
            P(),
            P(REQ, "mlp"),
            P(REQ, "mlp"),
            P("mlp", REQ),
        ),
        out_specs=P(REQ, "mlp"),
        check_vma=False,
    )
```
